1024 devices in a mesh: ctx: 64 (over z_hi, y, core), chan: 16 (over x, z_lo).
Axes of the slice: x: 4, y: 8, z: 16 (z_hi: 4, z_lo: 4; z = z_hi * 4 + z_lo), core: 2. Of those that a mesh axis runs over, the one named last changes fastest.
Arguments:
- query: bfloat16 [16384, 8192], P('ctx', 'chan'), may hold values from -6 to 6
- key_proj: bfloat16 [16384, 8192], P('ctx', 'chan'), may hold values from -6 to 6
- value: bfloat16 [16384, 8192], P('ctx', 'chan'), may hold values from -6 to 6
- residues: float32 [16, 8192], P(None, 'chan'), may hold values from -1.5 to 1.5
- rates: float32 [16, 8192], P(None, 'chan'), as said below
- cotangent: bfloat16 [16384, 8192], P('ctx', 'chan'), may hold values from -6 to 6
Outputs:
- output: bfloat16 [16384, 8192], P('ctx', 'chan')
- grad_query: bfloat16 [16384, 8192], P('ctx', 'chan')
- grad_key: bfloat16 [16384, 8192], P('ctx', 'chan')
- grad_value: bfloat16 [16384, 8192], P('ctx', 'chan')
The draws below stay inside these ranges and needn't reach their ends.
Inputs may be any that keep to these rules, and one draw needn't show every extreme that they name: `rates`: every rate is positive and at most 1/30.
All inputs are finite; a program needn't handle non-finite values.
Results may differ from the reference program's by a relative error of at most 0.0049.
Values sent between devices are 32-bit elements; how exact they have to be, the bound alone decides.
No kernel may reach another device: no remote copies, remote signals or barrier semaphores. Data moves between devices by JAX's collectives and lax.ppermute only.
A program may use at most 32 MiB of HBM per device.

```python
import math
import jax
import jax.numpy as jnp
from jax import lax

D = 8192
ORDER = 16
TOKENS = 16384


def draw_rates(key, part):
    upper = math.log(1.0 / 30.0)
    lower = math.log(0.3 / TOKENS)
    spread = jax.random.uniform(jax.random.fold_in(key, 11), (ORDER, D), dtype=jnp.float32)
    return jnp.exp(lower + (upper - lower) * spread)


def block_scale(own_key, extent, split, least, largest):
    level, own = 1.0, jax.random.fold_in(own_key, 6)
    for axis_at, shards_of in split:
        heights = jnp.exp(jax.random.uniform(jax.random.fold_in(own, axis_at), (shards_of,), jnp.float32, least / len(split), largest / len(split)))
        level = level * jnp.repeat(heights, extent[axis_at] // shards_of).reshape([-1 if axis == axis_at else 1 for axis in range(len(extent))])
    return level


def bell_draw(own_key, shape, scale, bound, split=(), kind=jnp.bfloat16):
    array = scale * jax.random.normal(own_key, shape, jnp.float32)
    if split:
        array = array * block_scale(own_key, shape, split, -0.22, 0.18)
    return jnp.clip(array, -bound, bound).astype(kind)


def setup_inputs(seed: int = 0) -> dict:
    streams_of = jax.random.split(jax.random.key(seed), 7)
    return {
        "query": bell_draw(streams_of[0], (TOKENS, D), 1.0, 6.0, ((0, 64), (1, 16))),
        "key_proj": bell_draw(streams_of[1], (TOKENS, D), 1.0, 6.0, ((0, 64), (1, 16))),
        "value": bell_draw(streams_of[2], (TOKENS, D), 1.0, 6.0, ((0, 64), (1, 16))),
        "residues": bell_draw(streams_of[3], (ORDER, D), 0.25, 1.5, ((1, 16),), jnp.float32),
        "rates": draw_rates(jax.random.fold_in(streams_of[6], 71), 0),
        "cotangent": bell_draw(streams_of[5], (TOKENS, D), 1.0, 6.0, ((0, 64), (1, 16))),
    }


def causal_conv(signal, residues, rates):
    size = 16
    width = signal.shape[1]
    scaled = residues * jnp.sqrt(-jnp.expm1(-2.0 * rates))
    lags = jnp.arange(size).astype(jnp.float32)
    powers = jnp.exp(-rates[None] * lags[:, None, None])
    kernel = lax.optimization_barrier(jnp.sum(scaled[None] * powers, axis=1))
    rows = jnp.arange(size)
    offset = rows[:, None] - rows[None, :]
    toeplitz = jnp.where((offset >= 0)[:, :, None], kernel[jnp.clip(offset, 0, size - 1)], 0.0)
    ends = jnp.exp(-rates[None] * (size - 1.0 - lags)[:, None, None])
    starts = jnp.exp(-rates[None] * (lags + 1.0)[:, None, None])
    block_decay = jnp.exp(-rates * size)
    blocks = signal.reshape(-1, size, width)

    def advance(state, block):
        inner = jnp.einsum('ijc,jc->ic', toeplitz, block, precision=lax.Precision.HIGHEST)
        carried = jnp.einsum('ikc,kc->ic', starts, scaled * state, precision=lax.Precision.HIGHEST)
        fresh = jnp.einsum('jkc,jc->kc', ends, block, precision=lax.Precision.HIGHEST)
        return (block_decay * state + fresh, inner + carried)
    _, pieces = lax.scan(advance, jnp.zeros(rates.shape, dtype=jnp.float32), blocks)
    return pieces.reshape(signal.shape)

def reference(query, key_proj, value, residues, rates, cotangent):
    query_f = query.astype(jnp.float32)
    key_f = key_proj.astype(jnp.float32)
    value_f = value.astype(jnp.float32)
    cot_f = cotangent.astype(jnp.float32)
    gated = lax.optimization_barrier((query_f * key_f).astype(jnp.bfloat16)).astype(jnp.float32)
    mixed = causal_conv(gated, residues, rates)
    output = (value_f * mixed).astype(jnp.bfloat16)
    grad_value = (cot_f * mixed).astype(jnp.bfloat16)
    weighted = cot_f * value_f
    back = causal_conv(weighted[::-1], residues, rates)[::-1]
    grad_query = (back * key_f).astype(jnp.bfloat16)
    grad_key = (back * query_f).astype(jnp.bfloat16)
    return (output, grad_query, grad_key, grad_value)
```

```python
import jax
import jax.numpy as jnp
from jax import lax
from jax.sharding import PartitionSpec as P

BLOCK = 64


def local_pass(signal, scaled, rates):
    length, width = signal.shape
    count = length // BLOCK
    order = rates.shape[0]
    lags = jnp.arange(BLOCK).astype(jnp.float32)
    rising = jnp.exp(rates[None] * lags[:, None, None])
    falling = jnp.exp(-rates[None] * lags[:, None, None])
    lower = (lags[:, None] >= lags[None, :]).astype(jnp.float32)
    step_decay = jnp.exp(-rates)

    def advance(state, block):
        lifted = (rising * block[:, None, :]).reshape(BLOCK, order * width)
        summed = jnp.dot(lower, lifted, precision=lax.Precision.HIGHEST).reshape(
            BLOCK, order, width
        )
        states = falling * (summed + step_decay * state[None])
        return (states[-1], jnp.sum(scaled[None] * states, axis=1))

    final, pieces = lax.scan(
        advance, jnp.zeros((order, width), jnp.float32), signal.reshape(count, BLOCK, width)
    )
    return (final, pieces)


def apply_incoming(pieces, incoming, scaled, rates):
    count = pieces.shape[0]
    lags = jnp.arange(BLOCK).astype(jnp.float32)
    after = jnp.exp(-rates[None] * (lags + 1.0)[:, None, None])
    block_index = jnp.arange(count).astype(jnp.float32)
    block_start = jnp.exp(-rates[None] * (BLOCK * block_index)[:, None, None])
    weights = block_start * (scaled * incoming)[None]
    extra = jnp.einsum("ikc,bkc->bic", after, weights, precision=lax.Precision.HIGHEST)
    return (pieces + extra).reshape(count * BLOCK, pieces.shape[2])


def incoming_states(local_state, rates, length, forward):
    count = lax.axis_size("ctx")

    def shift(carry, step):
        if forward:
            pairs = [(i, i + step) for i in range(count - step)]
        else:
            pairs = [(i + step, i) for i in range(count - step)]
        return lax.ppermute(carry, "ctx", pairs)

    carry = shift(local_state, 1)
    step = 1
    while step < count:
        carry = carry + jnp.exp(-rates * (length * step)) * shift(carry, step)
        step *= 2
    return carry


def per_device(query, key_proj, value, residues, rates, cotangent):
    length = query.shape[0]
    query_f = query.astype(jnp.float32)
    key_f = key_proj.astype(jnp.float32)
    value_f = value.astype(jnp.float32)
    cot_f = cotangent.astype(jnp.float32)
    scaled = residues * jnp.sqrt(-jnp.expm1(-2.0 * rates))
    gated = lax.optimization_barrier((query_f * key_f).astype(jnp.bfloat16)).astype(jnp.float32)
    weighted = cot_f * value_f
    fwd_state, fwd_pieces = local_pass(gated, scaled, rates)
    bwd_state, bwd_pieces = local_pass(weighted[::-1], scaled, rates)
    fwd_in = incoming_states(fwd_state, rates, length, True)
    bwd_in = incoming_states(bwd_state, rates, length, False)
    mixed = apply_incoming(fwd_pieces, fwd_in, scaled, rates)
    back = apply_incoming(bwd_pieces, bwd_in, scaled, rates)[::-1]
    output = (value_f * mixed).astype(jnp.bfloat16)
    grad_value = (cot_f * mixed).astype(jnp.bfloat16)
    grad_query = (back * key_f).astype(jnp.bfloat16)
    grad_key = (back * query_f).astype(jnp.bfloat16)
    return (output, grad_query, grad_key, grad_value)


def solution(mesh):
    return jax.shard_map(
        per_device,
        mesh=mesh,
        in_specs=(
            P("ctx", "chan"),
            P("ctx", "chan"),
            P("ctx", "chan"),
            P(None, "chan"),
            P(None, "chan"),
            P("ctx", "chan"),
        ),
        out_specs=(P("ctx", "chan"), P("ctx", "chan"), P("ctx", "chan"), P("ctx", "chan")),
        check_vma=False,
    )
```

```python
import jax
import jax.numpy as jnp
from jax import lax
from jax.sharding import PartitionSpec as P

BLOCK = 64


def local_pass(signal, scaled, rates):
    length, width = signal.shape
    count = length // BLOCK
    order = rates.shape[0]
    lags = jnp.arange(BLOCK).astype(jnp.float32)
    rising = jnp.exp(rates[None] * lags[:, None, None])
    falling = jnp.exp(-rates[None] * lags[:, None, None])
    lower = (lags[:, None] >= lags[None, :]).astype(jnp.float32)
    step_decay = jnp.exp(-rates)

    def advance(state, block):
        lifted = (rising * block[:, None, :]).reshape(BLOCK, order * width)
        summed = jnp.dot(lower, lifted, precision=lax.Precision.HIGHEST).reshape(
            BLOCK, order, width
        )
        states = falling * (summed + step_decay * state[None])
        return (states[-1], jnp.sum(scaled[None] * states, axis=1))

    final, pieces = lax.scan(
        advance, jnp.zeros((order, width), jnp.float32), signal.reshape(count, BLOCK, width)
    )
    return (final, pieces)


def apply_incoming(pieces, incoming, scaled, rates):
    count = pieces.shape[0]
    lags = jnp.arange(BLOCK).astype(jnp.float32)
    after = jnp.exp(-rates[None] * (lags + 1.0)[:, None, None])
    block_index = jnp.arange(count).astype(jnp.float32)
    block_start = jnp.exp(-rates[None] * (BLOCK * block_index)[:, None, None])
    weights = block_start * (scaled * incoming)[None]
    extra = jnp.einsum("ikc,bkc->bic", after, weights, precision=lax.Precision.HIGHEST)
    return (pieces + extra).reshape(count * BLOCK, pieces.shape[2])


def end_state(signal, rates):
    length, width = signal.shape
    part = 16
    lags = jnp.arange(part).astype(jnp.float32)
    inner = jnp.exp(-rates[None] * (part - 1.0 - lags)[:, None, None])
    outer = jnp.exp(-rates[None] * (part * (length // part - 1.0 - jnp.arange(length // part)))[:, None, None])
    rows = signal.reshape(length // part, part, 1, width)
    return jnp.sum(outer * jnp.sum(inner[None] * rows, axis=1), axis=0)


def incoming_states(fwd_state, bwd_state, rates, length, cover):
    count = lax.axis_size("ctx")
    radix = 4
    fwd_sum, bwd_sum = fwd_state, bwd_state
    fwd_in = jnp.zeros_like(fwd_state)
    bwd_in = jnp.zeros_like(bwd_state)
    span = 1
    while span < count:
        last = span * radix >= count
        fwd_next, bwd_next = fwd_sum, bwd_sum
        for k in range(1, radix):
            step = k * span
            if step >= count:
                break
            ahead = [(i, i + step) for i in range(count - step)]
            behind = [(i + step, i) for i in range(count - step)]
            fwd_got = lax.ppermute(fwd_sum, "ctx", ahead)
            bwd_got = lax.ppermute(bwd_sum, "ctx", behind)
            if last:
                fwd_got, bwd_got, cover = lax.optimization_barrier((fwd_got, bwd_got, cover))
            into = jnp.exp(-rates * (length * (step - 1.0)))
            fwd_in = fwd_in + into * fwd_got
            bwd_in = bwd_in + into * bwd_got
            if not last:
                past = jnp.exp(-rates * (length * step))
                fwd_next = fwd_next + past * fwd_got
                bwd_next = bwd_next + past * bwd_got
        fwd_sum, bwd_sum = fwd_next, bwd_next
        span *= radix
    return fwd_in, bwd_in, cover


def per_device(query, key_proj, value, residues, rates, cotangent):
    length = query.shape[0]
    query_f = query.astype(jnp.float32)
    key_f = key_proj.astype(jnp.float32)
    value_f = value.astype(jnp.float32)
    cot_f = cotangent.astype(jnp.float32)
    scaled = residues * jnp.sqrt(-jnp.expm1(-2.0 * rates))
    gated = lax.optimization_barrier((query_f * key_f).astype(jnp.bfloat16)).astype(jnp.float32)
    weighted = cot_f * value_f
    reversed_weighted = weighted[::-1]
    _, fwd_pieces = local_pass(gated, scaled, rates)
    _, bwd_pieces = local_pass(reversed_weighted, scaled, rates)
    fwd_in, bwd_in, (fwd_pieces, bwd_pieces) = incoming_states(
        end_state(gated, rates),
        end_state(reversed_weighted, rates),
        rates,
        length,
        (fwd_pieces, bwd_pieces),
    )
    mixed = apply_incoming(fwd_pieces, fwd_in, scaled, rates)
    back = apply_incoming(bwd_pieces, bwd_in, scaled, rates)[::-1]
    output = (value_f * mixed).astype(jnp.bfloat16)
    grad_value = (cot_f * mixed).astype(jnp.bfloat16)
    grad_query = (back * key_f).astype(jnp.bfloat16)
    grad_key = (back * query_f).astype(jnp.bfloat16)
    return (output, grad_query, grad_key, grad_value)


def solution(mesh):
    return jax.shard_map(
        per_device,
        mesh=mesh,
        in_specs=(
            P("ctx", "chan"),
            P("ctx", "chan"),
            P("ctx", "chan"),
            P(None, "chan"),
            P(None, "chan"),
            P("ctx", "chan"),
        ),
        out_specs=(P("ctx", "chan"), P("ctx", "chan"), P("ctx", "chan"), P("ctx", "chan")),
        check_vma=False,
    )
```

```python
import jax
import jax.numpy as jnp
from jax import lax
from jax.sharding import PartitionSpec as P

BLOCK = 64


def local_pass(signal, scaled, rates):
    length, width = signal.shape
    count = length // BLOCK
    order = rates.shape[0]
    lags = jnp.arange(BLOCK).astype(jnp.float32)
    rising = jnp.exp(rates[None] * lags[:, None, None])
    falling = jnp.exp(-rates[None] * lags[:, None, None])
    lower = (lags[:, None] >= lags[None, :]).astype(jnp.float32)
    step_decay = jnp.exp(-rates)

    def advance(state, block):
        lifted = (rising * block[:, None, :]).reshape(BLOCK, order * width)
        summed = jnp.dot(lower, lifted, precision=lax.Precision.HIGHEST).reshape(
            BLOCK, order, width
        )
        states = falling * (summed + step_decay * state[None])
        return (states[-1], jnp.sum(scaled[None] * states, axis=1))

    final, pieces = lax.scan(
        advance, jnp.zeros((order, width), jnp.float32), signal.reshape(count, BLOCK, width)
    )
    return (final, pieces)


def apply_incoming(pieces, incoming, scaled, rates):
    count = pieces.shape[0]
    lags = jnp.arange(BLOCK).astype(jnp.float32)
    after = jnp.exp(-rates[None] * (lags + 1.0)[:, None, None])
    block_index = jnp.arange(count).astype(jnp.float32)
    block_start = jnp.exp(-rates[None] * (BLOCK * block_index)[:, None, None])
    weights = block_start * (scaled * incoming)[None]
    extra = jnp.einsum("ikc,bkc->bic", after, weights, precision=lax.Precision.HIGHEST)
    return (pieces + extra).reshape(count * BLOCK, pieces.shape[2])


def end_state(signal, rates):
    length, width = signal.shape
    part = 16
    lags = jnp.arange(part).astype(jnp.float32)
    inner = jnp.exp(-rates[None] * (part - 1.0 - lags)[:, None, None])
    outer = jnp.exp(-rates[None] * (part * (length // part - 1.0 - jnp.arange(length // part)))[:, None, None])
    rows = signal.reshape(length // part, part, 1, width)
    return jnp.sum(outer * jnp.sum(inner[None] * rows, axis=1), axis=0)


def incoming_states(fwd_state, bwd_state, rates, length, cover):
    count = lax.axis_size("ctx")
    place = lax.axis_index("ctx")
    rounds = []
    span = 1
    while span < count:
        rounds.append(span)
        span *= 2
    slots = {rounds[min(2, len(rounds) - 1)]: 0, rounds[min(4, len(rounds) - 1)]: 1}
    cover = list(cover)
    fwd_total, bwd_total = fwd_state, bwd_state
    fwd_in = jnp.zeros_like(fwd_state)
    bwd_in = jnp.zeros_like(bwd_state)
    for span in rounds:
        got = lax.ppermute(
            jnp.stack([fwd_total, bwd_total]), "ctx", [(i, i ^ span) for i in range(count)]
        )
        if span in slots:
            got, cover[slots[span]] = lax.optimization_barrier((got, cover[slots[span]]))
        fwd_got, bwd_got = got[0], got[1]
        upper = (place // span) % 2 == 1
        offset = (place % span).astype(jnp.float32)
        fwd_in = fwd_in + jnp.where(upper, jnp.exp(-rates * (length * offset)), 0.0) * fwd_got
        bwd_in = bwd_in + jnp.where(
            upper, 0.0, jnp.exp(-rates * (length * (span - 1.0 - offset)))
        ) * bwd_got
        if 2 * span < count:
            whole = jnp.exp(-rates * (length * span))
            fwd_total = jnp.where(upper, whole * fwd_got + fwd_total, whole * fwd_total + fwd_got)
            bwd_total = jnp.where(upper, bwd_got + whole * bwd_total, bwd_total + whole * bwd_got)
    return fwd_in, bwd_in, tuple(cover)


def per_device(query, key_proj, value, residues, rates, cotangent):
    length = query.shape[0]
    query_f = query.astype(jnp.float32)
    key_f = key_proj.astype(jnp.float32)
    value_f = value.astype(jnp.float32)
    cot_f = cotangent.astype(jnp.float32)
    scaled = residues * jnp.sqrt(-jnp.expm1(-2.0 * rates))
    gated = lax.optimization_barrier((query_f * key_f).astype(jnp.bfloat16)).astype(jnp.float32)
    weighted = cot_f * value_f
    reversed_weighted = weighted[::-1]
    _, fwd_pieces = local_pass(gated, scaled, rates)
    _, bwd_pieces = local_pass(reversed_weighted, scaled, rates)
    fwd_in, bwd_in, (fwd_pieces, bwd_pieces) = incoming_states(
        end_state(gated, rates),
        end_state(reversed_weighted, rates),
        rates,
        length,
        (fwd_pieces, bwd_pieces),
    )
    mixed = apply_incoming(fwd_pieces, fwd_in, scaled, rates)
    back = apply_incoming(bwd_pieces, bwd_in, scaled, rates)[::-1]
    output = (value_f * mixed).astype(jnp.bfloat16)
    grad_value = (cot_f * mixed).astype(jnp.bfloat16)
    grad_query = (back * key_f).astype(jnp.bfloat16)
    grad_key = (back * query_f).astype(jnp.bfloat16)
    return (output, grad_query, grad_key, grad_value)


def solution(mesh):
    return jax.shard_map(
        per_device,
        mesh=mesh,
        in_specs=(
            P("ctx", "chan"),
            P("ctx", "chan"),
            P("ctx", "chan"),
            P(None, "chan"),
            P(None, "chan"),
            P("ctx", "chan"),
        ),
        out_specs=(P("ctx", "chan"), P("ctx", "chan"), P("ctx", "chan"), P("ctx", "chan")),
        check_vma=False,
    )
```

```python
import jax
import jax.numpy as jnp
from jax import lax
from jax.experimental import pallas as pl
from jax.sharding import PartitionSpec as P

BLOCK = 64


def local_kernel(signal_ref, scaled_ref, rates_ref, out_ref):
    length, width = signal_ref.shape
    order = rates_ref.shape[0]
    lags = lax.broadcasted_iota(jnp.int32, (BLOCK, width), 0).astype(jnp.float32)
    lower = (
        lax.broadcasted_iota(jnp.int32, (BLOCK, BLOCK), 0)
        >= lax.broadcasted_iota(jnp.int32, (BLOCK, BLOCK), 1)
    ).astype(jnp.float32)
    out_ref[...] = jnp.zeros(out_ref.shape, jnp.float32)

    def mode(m, carry):
        rate = rates_ref[pl.ds(m, 1), :]
        weight = scaled_ref[pl.ds(m, 1), :]
        rising = jnp.exp(rate * lags)
        falling = jnp.exp(-rate * lags)
        step_decay = jnp.exp(-rate)
        state = jnp.zeros((1, width), jnp.float32)
        for b in range(length // BLOCK):
            rows = pl.ds(b * BLOCK, BLOCK)
            summed = jnp.dot(
                lower,
                rising * signal_ref[rows, :],
                precision=lax.Precision.HIGHEST,
                preferred_element_type=jnp.float32,
            )
            states = falling * (summed + step_decay * state)
            out_ref[rows, :] += weight * states
            state = states[BLOCK - 1 : BLOCK, :]
        return carry

    lax.fori_loop(0, order, mode, 0)


def local_pass(signal, scaled, rates):
    length, width = signal.shape
    pieces = pl.pallas_call(
        local_kernel, out_shape=jax.ShapeDtypeStruct((length, width), jnp.float32)
    )(signal, scaled, rates)
    return pieces.reshape(length // BLOCK, BLOCK, width)


def apply_incoming(pieces, incoming, scaled, rates):
    count = pieces.shape[0]
    lags = jnp.arange(BLOCK).astype(jnp.float32)
    after = jnp.exp(-rates[None] * (lags + 1.0)[:, None, None])
    block_index = jnp.arange(count).astype(jnp.float32)
    block_start = jnp.exp(-rates[None] * (BLOCK * block_index)[:, None, None])
    weights = block_start * (scaled * incoming)[None]
    extra = jnp.einsum("ikc,bkc->bic", after, weights, precision=lax.Precision.HIGHEST)
    return (pieces + extra).reshape(count * BLOCK, pieces.shape[2])


def end_state(signal, rates):
    length, width = signal.shape
    part = 16
    lags = jnp.arange(part).astype(jnp.float32)
    inner = jnp.exp(-rates[None] * (part - 1.0 - lags)[:, None, None])
    outer = jnp.exp(-rates[None] * (part * (length // part - 1.0 - jnp.arange(length // part)))[:, None, None])
    rows = signal.reshape(length // part, part, 1, width)
    return jnp.sum(outer * jnp.sum(inner[None] * rows, axis=1), axis=0)


def incoming_states(fwd_state, bwd_state, rates, length, cover):
    count = lax.axis_size("ctx")
    place = lax.axis_index("ctx")
    rounds = []
    span = 1
    while span < count:
        rounds.append(span)
        span *= 2
    slots = {rounds[min(2, len(rounds) - 1)]: 0, rounds[min(4, len(rounds) - 1)]: 1}
    cover = list(cover)
    fwd_total, bwd_total = fwd_state, bwd_state
    fwd_in = jnp.zeros_like(fwd_state)
    bwd_in = jnp.zeros_like(bwd_state)
    for span in rounds:
        got = lax.ppermute(
            jnp.stack([fwd_total, bwd_total]), "ctx", [(i, i ^ span) for i in range(count)]
        )
        if span in slots:
            got, cover[slots[span]] = lax.optimization_barrier((got, cover[slots[span]]))
        fwd_got, bwd_got = got[0], got[1]
        upper = (place // span) % 2 == 1
        offset = (place % span).astype(jnp.float32)
        fwd_in = fwd_in + jnp.where(upper, jnp.exp(-rates * (length * offset)), 0.0) * fwd_got
        bwd_in = bwd_in + jnp.where(
            upper, 0.0, jnp.exp(-rates * (length * (span - 1.0 - offset)))
        ) * bwd_got
        if 2 * span < count:
            whole = jnp.exp(-rates * (length * span))
            fwd_total = jnp.where(upper, whole * fwd_got + fwd_total, whole * fwd_total + fwd_got)
            bwd_total = jnp.where(upper, bwd_got + whole * bwd_total, bwd_total + whole * bwd_got)
    return fwd_in, bwd_in, tuple(cover)


def per_device(query, key_proj, value, residues, rates, cotangent):
    length = query.shape[0]
    query_f = query.astype(jnp.float32)
    key_f = key_proj.astype(jnp.float32)
    value_f = value.astype(jnp.float32)
    cot_f = cotangent.astype(jnp.float32)
    scaled = residues * jnp.sqrt(-jnp.expm1(-2.0 * rates))
    gated = lax.optimization_barrier((query_f * key_f).astype(jnp.bfloat16)).astype(jnp.float32)
    weighted = cot_f * value_f
    reversed_weighted = weighted[::-1]
    fwd_pieces = local_pass(gated, scaled, rates)
    bwd_pieces = local_pass(reversed_weighted, scaled, rates)
    fwd_in, bwd_in, (fwd_pieces, bwd_pieces) = incoming_states(
        end_state(gated, rates),
        end_state(reversed_weighted, rates),
        rates,
        length,
        (fwd_pieces, bwd_pieces),
    )
    mixed = apply_incoming(fwd_pieces, fwd_in, scaled, rates)
    back = apply_incoming(bwd_pieces, bwd_in, scaled, rates)[::-1]
    output = (value_f * mixed).astype(jnp.bfloat16)
    grad_value = (cot_f * mixed).astype(jnp.bfloat16)
    grad_query = (back * key_f).astype(jnp.bfloat16)
    grad_key = (back * query_f).astype(jnp.bfloat16)
    return (output, grad_query, grad_key, grad_value)


def solution(mesh):
    return jax.shard_map(
        per_device,
        mesh=mesh,
        in_specs=(
            P("ctx", "chan"),
            P("ctx", "chan"),
            P("ctx", "chan"),
            P(None, "chan"),
            P(None, "chan"),
            P("ctx", "chan"),
        ),
        out_specs=(P("ctx", "chan"), P("ctx", "chan"), P("ctx", "chan"), P("ctx", "chan")),
        check_vma=False,
    )
```

```python
import jax
import jax.numpy as jnp
from jax import lax
from jax.experimental import pallas as pl
from jax.sharding import PartitionSpec as P

BLOCK = 64


def local_kernel(signal_ref, scaled_ref, rates_ref, out_ref):
    length, width = signal_ref.shape
    order = rates_ref.shape[0]
    lags = lax.broadcasted_iota(jnp.int32, (BLOCK, width), 0).astype(jnp.float32)
    lower = (
        lax.broadcasted_iota(jnp.int32, (BLOCK, BLOCK), 0)
        >= lax.broadcasted_iota(jnp.int32, (BLOCK, BLOCK), 1)
    ).astype(jnp.float32)
    out_ref[...] = jnp.zeros(out_ref.shape, jnp.float32)

    def mode(m, carry):
        rate = rates_ref[pl.ds(m, 1), :]
        weight = scaled_ref[pl.ds(m, 1), :]
        rising = jnp.exp(rate * lags)
        falling = jnp.exp(-rate * lags)
        step_decay = jnp.exp(-rate)
        state = jnp.zeros((1, width), jnp.float32)
        for b in range(length // BLOCK):
            rows = pl.ds(b * BLOCK, BLOCK)
            summed = jnp.dot(
                lower,
                rising * signal_ref[rows, :],
                precision=lax.Precision.HIGHEST,
                preferred_element_type=jnp.float32,
            )
            states = falling * (summed + step_decay * state)
            out_ref[rows, :] += weight * states
            state = states[BLOCK - 1 : BLOCK, :]
        return carry

    lax.fori_loop(0, order, mode, 0)


def local_pass(signal, scaled, rates):
    length, width = signal.shape
    pieces = pl.pallas_call(
        local_kernel, out_shape=jax.ShapeDtypeStruct((length, width), jnp.float32)
    )(signal, scaled, rates)
    return pieces.reshape(length // BLOCK, BLOCK, width)


def carried_kernel(weights_ref, rates_ref, out_ref):
    length, width = out_ref.shape
    order = rates_ref.shape[0]
    lags = lax.broadcasted_iota(jnp.int32, (BLOCK, width), 0).astype(jnp.float32) + 1.0
    out_ref[...] = jnp.zeros(out_ref.shape, jnp.float32)

    def mode(m, carry):
        rate = rates_ref[pl.ds(m, 1), :]
        weight = weights_ref[pl.ds(m, 1), :]
        after = jnp.exp(-rate * lags)
        for b in range(length // BLOCK):
            rows = pl.ds(b * BLOCK, BLOCK)
            out_ref[rows, :] += after * (weight * jnp.exp(-rate * float(b * BLOCK)))
        return carry

    lax.fori_loop(0, order, mode, 0)


def apply_incoming(pieces, incoming, scaled, rates):
    count, _, width = pieces.shape
    extra = pl.pallas_call(
        carried_kernel, out_shape=jax.ShapeDtypeStruct((count * BLOCK, width), jnp.float32)
    )(scaled * incoming, rates)
    return pieces.reshape(count * BLOCK, width) + extra


def end_state(signal, rates):
    length, width = signal.shape
    part = 16
    lags = jnp.arange(part).astype(jnp.float32)
    inner = jnp.exp(-rates[None] * (part - 1.0 - lags)[:, None, None])
    outer = jnp.exp(-rates[None] * (part * (length // part - 1.0 - jnp.arange(length // part)))[:, None, None])
    rows = signal.reshape(length // part, part, 1, width)
    return jnp.sum(outer * jnp.sum(inner[None] * rows, axis=1), axis=0)


def incoming_states(fwd_state, bwd_state, rates, length, cover):
    count = lax.axis_size("ctx")
    place = lax.axis_index("ctx")
    rounds = []
    span = 1
    while span < count:
        rounds.append(span)
        span *= 2
    slots = {rounds[min(2, len(rounds) - 1)]: 0, rounds[min(4, len(rounds) - 1)]: 1}
    cover = list(cover)
    fwd_total, bwd_total = fwd_state, bwd_state
    fwd_in = jnp.zeros_like(fwd_state)
    bwd_in = jnp.zeros_like(bwd_state)
    for span in rounds:
        got = lax.ppermute(
            jnp.stack([fwd_total, bwd_total]), "ctx", [(i, i ^ span) for i in range(count)]
        )
        if span in slots:
            got, cover[slots[span]] = lax.optimization_barrier((got, cover[slots[span]]))
        fwd_got, bwd_got = got[0], got[1]
        upper = (place // span) % 2 == 1
        offset = (place % span).astype(jnp.float32)
        fwd_in = fwd_in + jnp.where(upper, jnp.exp(-rates * (length * offset)), 0.0) * fwd_got
        bwd_in = bwd_in + jnp.where(
            upper, 0.0, jnp.exp(-rates * (length * (span - 1.0 - offset)))
        ) * bwd_got
        if 2 * span < count:
            whole = jnp.exp(-rates * (length * span))
            fwd_total = jnp.where(upper, whole * fwd_got + fwd_total, whole * fwd_total + fwd_got)
            bwd_total = jnp.where(upper, bwd_got + whole * bwd_total, bwd_total + whole * bwd_got)
    return fwd_in, bwd_in, tuple(cover)


def per_device(query, key_proj, value, residues, rates, cotangent):
    length = query.shape[0]
    query_f = query.astype(jnp.float32)
    key_f = key_proj.astype(jnp.float32)
    value_f = value.astype(jnp.float32)
    cot_f = cotangent.astype(jnp.float32)
    scaled = residues * jnp.sqrt(-jnp.expm1(-2.0 * rates))
    gated = lax.optimization_barrier((query_f * key_f).astype(jnp.bfloat16)).astype(jnp.float32)
    weighted = cot_f * value_f
    reversed_weighted = weighted[::-1]
    fwd_pieces = local_pass(gated, scaled, rates)
    bwd_pieces = local_pass(reversed_weighted, scaled, rates)
    fwd_in, bwd_in, (fwd_pieces, bwd_pieces) = incoming_states(
        end_state(gated, rates),
        end_state(reversed_weighted, rates),
        rates,
        length,
        (fwd_pieces, bwd_pieces),
    )
    mixed = apply_incoming(fwd_pieces, fwd_in, scaled, rates)
    back = apply_incoming(bwd_pieces, bwd_in, scaled, rates)[::-1]
    output = (value_f * mixed).astype(jnp.bfloat16)
    grad_value = (cot_f * mixed).astype(jnp.bfloat16)
    grad_query = (back * key_f).astype(jnp.bfloat16)
    grad_key = (back * query_f).astype(jnp.bfloat16)
    return (output, grad_query, grad_key, grad_value)


def solution(mesh):
    return jax.shard_map(
        per_device,
        mesh=mesh,
        in_specs=(
            P("ctx", "chan"),
            P("ctx", "chan"),
            P("ctx", "chan"),
            P(None, "chan"),
            P(None, "chan"),
            P("ctx", "chan"),
        ),
        out_specs=(P("ctx", "chan"), P("ctx", "chan"), P("ctx", "chan"), P("ctx", "chan")),
        check_vma=False,
    )
```

```python
import jax
import jax.numpy as jnp
from jax import lax
from jax.experimental import pallas as pl
from jax.sharding import PartitionSpec as P

BLOCK = 64


def local_kernel(signal_ref, scaled_ref, rates_ref, out_ref):
    length, width = signal_ref.shape
    order = rates_ref.shape[0]
    lags = lax.broadcasted_iota(jnp.int32, (BLOCK, width), 0).astype(jnp.float32)
    lower = (
        lax.broadcasted_iota(jnp.int32, (BLOCK, BLOCK), 0)
        >= lax.broadcasted_iota(jnp.int32, (BLOCK, BLOCK), 1)
    ).astype(jnp.float32)
    out_ref[...] = jnp.zeros(out_ref.shape, jnp.float32)

    def mode(m, carry):
        rate = rates_ref[pl.ds(m, 1), :]
        weight = scaled_ref[pl.ds(m, 1), :]
        rising = jnp.exp(rate * lags)
        falling = jnp.exp(-rate * lags)
        step_decay = jnp.exp(-rate)
        state = jnp.zeros((1, width), jnp.float32)
        for b in range(length // BLOCK):
            rows = pl.ds(b * BLOCK, BLOCK)
            summed = jnp.dot(
                lower,
                rising * signal_ref[rows, :],
                precision=lax.Precision.HIGHEST,
                preferred_element_type=jnp.float32,
            )
            states = falling * (summed + step_decay * state)
            out_ref[rows, :] += weight * states
            state = states[BLOCK - 1 : BLOCK, :]
        return carry

    lax.fori_loop(0, order, mode, 0)


def local_pass(signal, scaled, rates):
    length, width = signal.shape
    pieces = pl.pallas_call(
        local_kernel, out_shape=jax.ShapeDtypeStruct((length, width), jnp.float32)
    )(signal, scaled, rates)
    return pieces.reshape(length // BLOCK, BLOCK, width)


def carried_kernel(weights_ref, rates_ref, out_ref):
    length, width = out_ref.shape
    order = rates_ref.shape[0]
    lags = lax.broadcasted_iota(jnp.int32, (BLOCK, width), 0).astype(jnp.float32) + 1.0
    out_ref[...] = jnp.zeros(out_ref.shape, jnp.float32)

    def mode(m, carry):
        rate = rates_ref[pl.ds(m, 1), :]
        weight = weights_ref[pl.ds(m, 1), :]
        after = jnp.exp(-rate * lags)
        for b in range(length // BLOCK):
            rows = pl.ds(b * BLOCK, BLOCK)
            out_ref[rows, :] += after * (weight * jnp.exp(-rate * float(b * BLOCK)))
        return carry

    lax.fori_loop(0, order, mode, 0)


def apply_incoming(pieces, incoming, scaled, rates):
    count, _, width = pieces.shape
    extra = pl.pallas_call(
        carried_kernel, out_shape=jax.ShapeDtypeStruct((count * BLOCK, width), jnp.float32)
    )(scaled * incoming, rates)
    return pieces.reshape(count * BLOCK, width) + extra


def end_state(signal, rates):
    length, width = signal.shape
    part = 16
    lags = jnp.arange(part).astype(jnp.float32)
    inner = jnp.exp(-rates[None] * (part - 1.0 - lags)[:, None, None])
    outer = jnp.exp(-rates[None] * (part * (length // part - 1.0 - jnp.arange(length // part)))[:, None, None])
    rows = signal.reshape(length // part, part, 1, width)
    return jnp.sum(outer * jnp.sum(inner[None] * rows, axis=1), axis=0)


RINGS = (4, 8, 2)


def partner(place, span, count):
    sizes = RINGS if count == 4 * 8 * 2 else (count,)
    inner = count
    for size in sizes:
        inner //= size
        coord = (place // inner) % size
        if span < inner or span >= inner * size:
            continue
        bit = span // inner
        if size >= 4 and bit == size // 2:
            quarter = size // 4
            moved = coord + quarter if (coord // quarter) % 2 == 1 else coord - quarter
            return place + ((moved % size) - coord) * inner
        return place ^ span
    return place ^ span


def incoming_states(fwd_state, bwd_state, rates, length, cover):
    count = lax.axis_size("ctx")
    place = lax.axis_index("ctx")
    rounds = []
    span = 1
    while span < count:
        rounds.append(span)
        span *= 2
    slots = {rounds[min(2, len(rounds) - 1)]: 0, rounds[min(4, len(rounds) - 1)]: 1}
    cover = list(cover)
    fwd_total, bwd_total = fwd_state, bwd_state
    fwd_in = jnp.zeros_like(fwd_state)
    bwd_in = jnp.zeros_like(bwd_state)
    for span in rounds:
        got = lax.ppermute(
            jnp.stack([fwd_total, bwd_total]),
            "ctx",
            [(i, partner(i, span, count)) for i in range(count)],
        )
        if span in slots:
            got, cover[slots[span]] = lax.optimization_barrier((got, cover[slots[span]]))
        fwd_got, bwd_got = got[0], got[1]
        upper = (place // span) % 2 == 1
        offset = (place % span).astype(jnp.float32)
        fwd_in = fwd_in + jnp.where(upper, jnp.exp(-rates * (length * offset)), 0.0) * fwd_got
        bwd_in = bwd_in + jnp.where(
            upper, 0.0, jnp.exp(-rates * (length * (span - 1.0 - offset)))
        ) * bwd_got
        if 2 * span < count:
            whole = jnp.exp(-rates * (length * span))
            fwd_total = jnp.where(upper, whole * fwd_got + fwd_total, whole * fwd_total + fwd_got)
            bwd_total = jnp.where(upper, bwd_got + whole * bwd_total, bwd_total + whole * bwd_got)
    return fwd_in, bwd_in, tuple(cover)


def per_device(query, key_proj, value, residues, rates, cotangent):
    length = query.shape[0]
    query_f = query.astype(jnp.float32)
    key_f = key_proj.astype(jnp.float32)
    value_f = value.astype(jnp.float32)
    cot_f = cotangent.astype(jnp.float32)
    scaled = residues * jnp.sqrt(-jnp.expm1(-2.0 * rates))
    gated = lax.optimization_barrier((query_f * key_f).astype(jnp.bfloat16)).astype(jnp.float32)
    weighted = cot_f * value_f
    reversed_weighted = weighted[::-1]
    fwd_pieces = local_pass(gated, scaled, rates)
    bwd_pieces = local_pass(reversed_weighted, scaled, rates)
    fwd_in, bwd_in, (fwd_pieces, bwd_pieces) = incoming_states(
        end_state(gated, rates),
        end_state(reversed_weighted, rates),
        rates,
        length,
        (fwd_pieces, bwd_pieces),
    )
    mixed = apply_incoming(fwd_pieces, fwd_in, scaled, rates)
    back = apply_incoming(bwd_pieces, bwd_in, scaled, rates)[::-1]
    output = (value_f * mixed).astype(jnp.bfloat16)
    grad_value = (cot_f * mixed).astype(jnp.bfloat16)
    grad_query = (back * key_f).astype(jnp.bfloat16)
    grad_key = (back * query_f).astype(jnp.bfloat16)
    return (output, grad_query, grad_key, grad_value)


def solution(mesh):
    return jax.shard_map(
        per_device,
        mesh=mesh,
        in_specs=(
            P("ctx", "chan"),
            P("ctx", "chan"),
            P("ctx", "chan"),
            P(None, "chan"),
            P(None, "chan"),
            P("ctx", "chan"),
        ),
        out_specs=(P("ctx", "chan"), P("ctx", "chan"), P("ctx", "chan"), P("ctx", "chan")),
        check_vma=False,
    )
```

```python
import jax
import jax.numpy as jnp
from jax import lax
from jax.experimental import pallas as pl
from jax.sharding import PartitionSpec as P

BLOCK = 64


def local_kernel(signal_ref, scaled_ref, rates_ref, out_ref):
    length, width = signal_ref.shape
    order = rates_ref.shape[0]
    lags = lax.broadcasted_iota(jnp.int32, (BLOCK, width), 0).astype(jnp.float32)
    lower = (
        lax.broadcasted_iota(jnp.int32, (BLOCK, BLOCK), 0)
        >= lax.broadcasted_iota(jnp.int32, (BLOCK, BLOCK), 1)
    ).astype(jnp.float32)
    out_ref[...] = jnp.zeros(out_ref.shape, jnp.float32)

    def mode(m, carry):
        rate = rates_ref[pl.ds(m, 1), :]
        weight = scaled_ref[pl.ds(m, 1), :]
        rising = jnp.exp(rate * lags)
        falling = jnp.exp(-rate * lags)
        step_decay = jnp.exp(-rate)
        state = jnp.zeros((1, width), jnp.float32)
        for b in range(length // BLOCK):
            rows = pl.ds(b * BLOCK, BLOCK)
            summed = jnp.dot(
                lower,
                rising * signal_ref[rows, :],
                precision=lax.Precision.HIGHEST,
                preferred_element_type=jnp.float32,
            )
            states = falling * (summed + step_decay * state)
            out_ref[rows, :] += weight * states
            state = states[BLOCK - 1 : BLOCK, :]
        return carry

    lax.fori_loop(0, order, mode, 0)


def local_pass(signal, scaled, rates):
    length, width = signal.shape
    pieces = pl.pallas_call(
        local_kernel, out_shape=jax.ShapeDtypeStruct((length, width), jnp.float32)
    )(signal, scaled, rates)
    return pieces.reshape(length // BLOCK, BLOCK, width)


def carried_kernel(weights_ref, rates_ref, out_ref):
    length, width = out_ref.shape
    order = rates_ref.shape[0]
    lags = lax.broadcasted_iota(jnp.int32, (BLOCK, width), 0).astype(jnp.float32) + 1.0
    out_ref[...] = jnp.zeros(out_ref.shape, jnp.float32)

    def mode(m, carry):
        rate = rates_ref[pl.ds(m, 1), :]
        weight = weights_ref[pl.ds(m, 1), :]
        after = jnp.exp(-rate * lags)
        for b in range(length // BLOCK):
            rows = pl.ds(b * BLOCK, BLOCK)
            out_ref[rows, :] += after * (weight * jnp.exp(-rate * float(b * BLOCK)))
        return carry

    lax.fori_loop(0, order, mode, 0)


def apply_incoming(pieces, incoming, scaled, rates):
    count, _, width = pieces.shape
    extra = pl.pallas_call(
        carried_kernel, out_shape=jax.ShapeDtypeStruct((count * BLOCK, width), jnp.float32)
    )(scaled * incoming, rates)
    return pieces.reshape(count * BLOCK, width) + extra


def end_state(signal, rates):
    length, width = signal.shape
    part = 16
    lags = jnp.arange(part).astype(jnp.float32)
    inner = jnp.exp(-rates[None] * (part - 1.0 - lags)[:, None, None])
    outer = jnp.exp(-rates[None] * (part * (length // part - 1.0 - jnp.arange(length // part)))[:, None, None])
    rows = signal.reshape(length // part, part, 1, width)
    return jnp.sum(outer * jnp.sum(inner[None] * rows, axis=1), axis=0)


RINGS = (4, 8, 2)


def partner(place, span, count):
    sizes = RINGS if count == 4 * 8 * 2 else (count,)
    inner = count
    for size in sizes:
        inner //= size
        coord = (place // inner) % size
        if span < inner or span >= inner * size:
            continue
        bit = span // inner
        if size >= 4 and bit == size // 2:
            quarter = size // 4
            moved = coord + quarter if (coord // quarter) % 2 == 1 else coord - quarter
            return place + ((moved % size) - coord) * inner
        return place ^ span
    return place ^ span


def incoming_states(fwd_state, bwd_state, rates, length, cover):
    count = lax.axis_size("ctx")
    place = lax.axis_index("ctx")
    rounds = []
    span = 1
    while span < count:
        rounds.append(span)
        span *= 2
    slots = {span: k for k, span in enumerate(rounds[len(rounds) - len(cover) :])}
    cover = list(cover)
    fwd_total, bwd_total = fwd_state, bwd_state
    fwd_in = jnp.zeros_like(fwd_state)
    bwd_in = jnp.zeros_like(bwd_state)
    for span in rounds:
        got = lax.ppermute(
            jnp.stack([fwd_total, bwd_total]),
            "ctx",
            [(i, partner(i, span, count)) for i in range(count)],
        )
        if span in slots:
            got, cover[slots[span]] = lax.optimization_barrier((got, cover[slots[span]]))
        fwd_got, bwd_got = got[0], got[1]
        upper = (place // span) % 2 == 1
        offset = (place % span).astype(jnp.float32)
        fwd_in = fwd_in + jnp.where(upper, jnp.exp(-rates * (length * offset)), 0.0) * fwd_got
        bwd_in = bwd_in + jnp.where(
            upper, 0.0, jnp.exp(-rates * (length * (span - 1.0 - offset)))
        ) * bwd_got
        if 2 * span < count:
            whole = jnp.exp(-rates * (length * span))
            fwd_total = jnp.where(upper, whole * fwd_got + fwd_total, whole * fwd_total + fwd_got)
            bwd_total = jnp.where(upper, bwd_got + whole * bwd_total, bwd_total + whole * bwd_got)
    return fwd_in, bwd_in, tuple(cover)


def per_device(query, key_proj, value, residues, rates, cotangent):
    length = query.shape[0]
    query_f = query.astype(jnp.float32)
    key_f = key_proj.astype(jnp.float32)
    value_f = value.astype(jnp.float32)
    cot_f = cotangent.astype(jnp.float32)
    scaled = residues * jnp.sqrt(-jnp.expm1(-2.0 * rates))
    gated = lax.optimization_barrier((query_f * key_f).astype(jnp.bfloat16)).astype(jnp.float32)
    weighted = cot_f * value_f
    reversed_weighted = weighted[::-1]
    half = rates.shape[0] // 2
    cover = tuple(
        local_pass(signal, scaled[modes], rates[modes])
        for signal in (gated, reversed_weighted)
        for modes in (slice(0, half), slice(half, None))
    )
    fwd_in, bwd_in, cover = incoming_states(
        end_state(gated, rates),
        end_state(reversed_weighted, rates),
        rates,
        length,
        cover,
    )
    fwd_pieces = cover[0] + cover[1]
    bwd_pieces = cover[2] + cover[3]
    mixed = apply_incoming(fwd_pieces, fwd_in, scaled, rates)
    back = apply_incoming(bwd_pieces, bwd_in, scaled, rates)[::-1]
    output = (value_f * mixed).astype(jnp.bfloat16)
    grad_value = (cot_f * mixed).astype(jnp.bfloat16)
    grad_query = (back * key_f).astype(jnp.bfloat16)
    grad_key = (back * query_f).astype(jnp.bfloat16)
    return (output, grad_query, grad_key, grad_value)


def solution(mesh):
    return jax.shard_map(
        per_device,
        mesh=mesh,
        in_specs=(
            P("ctx", "chan"),
            P("ctx", "chan"),
            P("ctx", "chan"),
            P(None, "chan"),
            P(None, "chan"),
            P("ctx", "chan"),
        ),
        out_specs=(P("ctx", "chan"), P("ctx", "chan"), P("ctx", "chan"), P("ctx", "chan")),
        check_vma=False,
    )
```

```python
import jax
import jax.numpy as jnp
from jax import lax
from jax.experimental import pallas as pl
from jax.sharding import PartitionSpec as P

BLOCK = 64


def local_kernel(signal_ref, scaled_ref, rates_ref, out_ref):
    length, width = signal_ref.shape
    order = rates_ref.shape[0]
    lags = lax.broadcasted_iota(jnp.int32, (BLOCK, width), 0).astype(jnp.float32)
    lower = (
        lax.broadcasted_iota(jnp.int32, (BLOCK, BLOCK), 0)
        >= lax.broadcasted_iota(jnp.int32, (BLOCK, BLOCK), 1)
    ).astype(jnp.float32)
    out_ref[...] = jnp.zeros(out_ref.shape, jnp.float32)

    def mode(m, carry):
        rate = rates_ref[pl.ds(m, 1), :]
        weight = scaled_ref[pl.ds(m, 1), :]
        rising = jnp.exp(rate * lags)
        falling = jnp.exp(-rate * lags)
        step_decay = jnp.exp(-rate)
        state = jnp.zeros((1, width), jnp.float32)
        for b in range(length // BLOCK):
            rows = pl.ds(b * BLOCK, BLOCK)
            summed = jnp.dot(
                lower,
                rising * signal_ref[rows, :],
                precision=lax.Precision.HIGHEST,
                preferred_element_type=jnp.float32,
            )
            states = falling * (summed + step_decay * state)
            out_ref[rows, :] += weight * states
            state = states[BLOCK - 1 : BLOCK, :]
        return carry

    lax.fori_loop(0, order, mode, 0)


def local_pass(signal, scaled, rates):
    length, width = signal.shape
    pieces = pl.pallas_call(
        local_kernel, out_shape=jax.ShapeDtypeStruct((length, width), jnp.float32)
    )(signal, scaled, rates)
    return pieces.reshape(length // BLOCK, BLOCK, width)


def carried_kernel(fwd_ref, bwd_ref, scaled_ref, rates_ref, fwd_out, bwd_out):
    length, width = fwd_out.shape
    order = rates_ref.shape[0]
    lags = lax.broadcasted_iota(jnp.int32, (BLOCK, width), 0).astype(jnp.float32) + 1.0
    fwd_out[...] = jnp.zeros(fwd_out.shape, jnp.float32)
    bwd_out[...] = jnp.zeros(bwd_out.shape, jnp.float32)

    def mode(m, carry):
        rate = rates_ref[pl.ds(m, 1), :]
        weight = scaled_ref[pl.ds(m, 1), :]
        fwd_weight = weight * fwd_ref[pl.ds(m, 1), :]
        bwd_weight = weight * bwd_ref[pl.ds(m, 1), :]
        after = jnp.exp(-rate * lags)
        for b in range(length // BLOCK):
            rows = pl.ds(b * BLOCK, BLOCK)
            start = jnp.exp(-rate * float(b * BLOCK))
            fwd_out[rows, :] += after * (fwd_weight * start)
            bwd_out[rows, :] += after * (bwd_weight * start)
        return carry

    lax.fori_loop(0, order, mode, 0)


def carried(fwd_in, bwd_in, scaled, rates, length):
    shape = jax.ShapeDtypeStruct((length, fwd_in.shape[1]), jnp.float32)
    return pl.pallas_call(carried_kernel, out_shape=(shape, shape))(fwd_in, bwd_in, scaled, rates)


def end_state(signal, rates):
    length, width = signal.shape
    part = 16
    lags = jnp.arange(part).astype(jnp.float32)
    inner = jnp.exp(-rates[None] * (part - 1.0 - lags)[:, None, None])
    outer = jnp.exp(-rates[None] * (part * (length // part - 1.0 - jnp.arange(length // part)))[:, None, None])
    rows = signal.reshape(length // part, part, 1, width)
    return jnp.sum(outer * jnp.sum(inner[None] * rows, axis=1), axis=0)


RINGS = (4, 8, 2)


def partner(place, span, count):
    sizes = RINGS if count == 4 * 8 * 2 else (count,)
    inner = count
    for size in sizes:
        inner //= size
        coord = (place // inner) % size
        if span < inner or span >= inner * size:
            continue
        bit = span // inner
        if size >= 4 and bit == size // 2:
            quarter = size // 4
            moved = coord + quarter if (coord // quarter) % 2 == 1 else coord - quarter
            return place + ((moved % size) - coord) * inner
        return place ^ span
    return place ^ span


def incoming_states(fwd_state, bwd_state, rates, length, cover):
    count = lax.axis_size("ctx")
    place = lax.axis_index("ctx")
    rounds = []
    span = 1
    while span < count:
        rounds.append(span)
        span *= 2
    slots = {span: k for k, span in enumerate(rounds[len(rounds) - len(cover) :])}
    cover = list(cover)
    fwd_total, bwd_total = fwd_state, bwd_state
    fwd_in = jnp.zeros_like(fwd_state)
    bwd_in = jnp.zeros_like(bwd_state)
    for span in rounds:
        got = lax.ppermute(
            jnp.stack([fwd_total, bwd_total]),
            "ctx",
            [(i, partner(i, span, count)) for i in range(count)],
        )
        if span in slots:
            got, cover[slots[span]] = lax.optimization_barrier((got, cover[slots[span]]))
        fwd_got, bwd_got = got[0], got[1]
        upper = (place // span) % 2 == 1
        offset = (place % span).astype(jnp.float32)
        fwd_in = fwd_in + jnp.where(upper, jnp.exp(-rates * (length * offset)), 0.0) * fwd_got
        bwd_in = bwd_in + jnp.where(
            upper, 0.0, jnp.exp(-rates * (length * (span - 1.0 - offset)))
        ) * bwd_got
        if 2 * span < count:
            whole = jnp.exp(-rates * (length * span))
            fwd_total = jnp.where(upper, whole * fwd_got + fwd_total, whole * fwd_total + fwd_got)
            bwd_total = jnp.where(upper, bwd_got + whole * bwd_total, bwd_total + whole * bwd_got)
    return fwd_in, bwd_in, tuple(cover)


def per_device(query, key_proj, value, residues, rates, cotangent):
    length = query.shape[0]
    query_f = query.astype(jnp.float32)
    key_f = key_proj.astype(jnp.float32)
    value_f = value.astype(jnp.float32)
    cot_f = cotangent.astype(jnp.float32)
    scaled = residues * jnp.sqrt(-jnp.expm1(-2.0 * rates))
    gated = lax.optimization_barrier((query_f * key_f).astype(jnp.bfloat16)).astype(jnp.float32)
    weighted = cot_f * value_f
    reversed_weighted = weighted[::-1]
    half = rates.shape[0] // 2
    cover = tuple(
        local_pass(signal, scaled[modes], rates[modes])
        for signal in (gated, reversed_weighted)
        for modes in (slice(0, half), slice(half, None))
    )
    fwd_in, bwd_in, cover = incoming_states(
        end_state(gated, rates),
        end_state(reversed_weighted, rates),
        rates,
        length,
        cover,
    )
    fwd_pieces = cover[0] + cover[1]
    bwd_pieces = cover[2] + cover[3]
    fwd_extra, bwd_extra = carried(fwd_in, bwd_in, scaled, rates, length)
    mixed = fwd_pieces.reshape(length, -1) + fwd_extra
    back = (bwd_pieces.reshape(length, -1) + bwd_extra)[::-1]
    output = (value_f * mixed).astype(jnp.bfloat16)
    grad_value = (cot_f * mixed).astype(jnp.bfloat16)
    grad_query = (back * key_f).astype(jnp.bfloat16)
    grad_key = (back * query_f).astype(jnp.bfloat16)
    return (output, grad_query, grad_key, grad_value)


def solution(mesh):
    return jax.shard_map(
        per_device,
        mesh=mesh,
        in_specs=(
            P("ctx", "chan"),
            P("ctx", "chan"),
            P("ctx", "chan"),
            P(None, "chan"),
            P(None, "chan"),
            P("ctx", "chan"),
        ),
        out_specs=(P("ctx", "chan"), P("ctx", "chan"), P("ctx", "chan"), P("ctx", "chan")),
        check_vma=False,
    )
```

```python
import jax
import jax.numpy as jnp
from jax import lax
from jax.experimental import pallas as pl
from jax.sharding import PartitionSpec as P

BLOCK = 64


def local_kernel(signal_ref, scaled_ref, rates_ref, out_ref):
    length, width = signal_ref.shape
    order = rates_ref.shape[0]
    lags = lax.broadcasted_iota(jnp.int32, (BLOCK, width), 0).astype(jnp.float32)
    lower = (
        lax.broadcasted_iota(jnp.int32, (BLOCK, BLOCK), 0)
        >= lax.broadcasted_iota(jnp.int32, (BLOCK, BLOCK), 1)
    ).astype(jnp.bfloat16)
    out_ref[...] = jnp.zeros(out_ref.shape, jnp.float32)

    def mode(m, carry):
        rate = rates_ref[pl.ds(m, 1), :]
        weight = scaled_ref[pl.ds(m, 1), :]
        rising = jnp.exp(rate * lags)
        falling = jnp.exp(-rate * lags)
        step_decay = jnp.exp(-rate)
        state = jnp.zeros((1, width), jnp.float32)
        for b in range(length // BLOCK):
            rows = pl.ds(b * BLOCK, BLOCK)
            lifted = rising * signal_ref[rows, :]
            high = lifted.astype(jnp.bfloat16)
            low = (lifted - high.astype(jnp.float32)).astype(jnp.bfloat16)
            summed = jnp.dot(lower, high, preferred_element_type=jnp.float32) + jnp.dot(
                lower, low, preferred_element_type=jnp.float32
            )
            states = falling * (summed + step_decay * state)
            out_ref[rows, :] += weight * states
            state = states[BLOCK - 1 : BLOCK, :]
        return carry

    lax.fori_loop(0, order, mode, 0)


def local_pass(signal, scaled, rates):
    length, width = signal.shape
    pieces = pl.pallas_call(
        local_kernel, out_shape=jax.ShapeDtypeStruct((length, width), jnp.float32)
    )(signal, scaled, rates)
    return pieces.reshape(length // BLOCK, BLOCK, width)


def carried_kernel(fwd_ref, bwd_ref, scaled_ref, rates_ref, fwd_out, bwd_out):
    length, width = fwd_out.shape
    order = rates_ref.shape[0]
    lags = lax.broadcasted_iota(jnp.int32, (BLOCK, width), 0).astype(jnp.float32) + 1.0
    fwd_out[...] = jnp.zeros(fwd_out.shape, jnp.float32)
    bwd_out[...] = jnp.zeros(bwd_out.shape, jnp.float32)

    def mode(m, carry):
        rate = rates_ref[pl.ds(m, 1), :]
        weight = scaled_ref[pl.ds(m, 1), :]
        fwd_weight = weight * fwd_ref[pl.ds(m, 1), :]
        bwd_weight = weight * bwd_ref[pl.ds(m, 1), :]
        after = jnp.exp(-rate * lags)
        for b in range(length // BLOCK):
            rows = pl.ds(b * BLOCK, BLOCK)
            start = jnp.exp(-rate * float(b * BLOCK))
            fwd_out[rows, :] += after * (fwd_weight * start)
            bwd_out[rows, :] += after * (bwd_weight * start)
        return carry

    lax.fori_loop(0, order, mode, 0)


def carried(fwd_in, bwd_in, scaled, rates, length):
    shape = jax.ShapeDtypeStruct((length, fwd_in.shape[1]), jnp.float32)
    return pl.pallas_call(carried_kernel, out_shape=(shape, shape))(fwd_in, bwd_in, scaled, rates)


def end_state(signal, rates):
    length, width = signal.shape
    part = 16
    lags = jnp.arange(part).astype(jnp.float32)
    inner = jnp.exp(-rates[None] * (part - 1.0 - lags)[:, None, None])
    outer = jnp.exp(-rates[None] * (part * (length // part - 1.0 - jnp.arange(length // part)))[:, None, None])
    rows = signal.reshape(length // part, part, 1, width)
    return jnp.sum(outer * jnp.sum(inner[None] * rows, axis=1), axis=0)


RINGS = (4, 8, 2)


def partner(place, span, count):
    sizes = RINGS if count == 4 * 8 * 2 else (count,)
    inner = count
    for size in sizes:
        inner //= size
        coord = (place // inner) % size
        if span < inner or span >= inner * size:
            continue
        bit = span // inner
        if size >= 4 and bit == size // 2:
            quarter = size // 4
            moved = coord + quarter if (coord // quarter) % 2 == 1 else coord - quarter
            return place + ((moved % size) - coord) * inner
        return place ^ span
    return place ^ span


def incoming_states(fwd_state, bwd_state, rates, length, cover):
    count = lax.axis_size("ctx")
    place = lax.axis_index("ctx")
    rounds = []
    span = 1
    while span < count:
        rounds.append(span)
        span *= 2
    slots = {span: k for k, span in enumerate(rounds[len(rounds) - len(cover) :])}
    cover = list(cover)
    fwd_total, bwd_total = fwd_state, bwd_state
    fwd_in = jnp.zeros_like(fwd_state)
    bwd_in = jnp.zeros_like(bwd_state)
    for span in rounds:
        got = lax.ppermute(
            jnp.stack([fwd_total, bwd_total]),
            "ctx",
            [(i, partner(i, span, count)) for i in range(count)],
        )
        if span in slots:
            got, cover[slots[span]] = lax.optimization_barrier((got, cover[slots[span]]))
        fwd_got, bwd_got = got[0], got[1]
        upper = (place // span) % 2 == 1
        offset = (place % span).astype(jnp.float32)
        fwd_in = fwd_in + jnp.where(upper, jnp.exp(-rates * (length * offset)), 0.0) * fwd_got
        bwd_in = bwd_in + jnp.where(
            upper, 0.0, jnp.exp(-rates * (length * (span - 1.0 - offset)))
        ) * bwd_got
        if 2 * span < count:
            whole = jnp.exp(-rates * (length * span))
            fwd_total = jnp.where(upper, whole * fwd_got + fwd_total, whole * fwd_total + fwd_got)
            bwd_total = jnp.where(upper, bwd_got + whole * bwd_total, bwd_total + whole * bwd_got)
    return fwd_in, bwd_in, tuple(cover)


def per_device(query, key_proj, value, residues, rates, cotangent):
    length = query.shape[0]
    query_f = query.astype(jnp.float32)
    key_f = key_proj.astype(jnp.float32)
    value_f = value.astype(jnp.float32)
    cot_f = cotangent.astype(jnp.float32)
    scaled = residues * jnp.sqrt(-jnp.expm1(-2.0 * rates))
    gated = lax.optimization_barrier((query_f * key_f).astype(jnp.bfloat16)).astype(jnp.float32)
    weighted = cot_f * value_f
    reversed_weighted = weighted[::-1]
    half = rates.shape[0] // 2
    cover = tuple(
        local_pass(signal, scaled[modes], rates[modes])
        for signal in (gated, reversed_weighted)
        for modes in (slice(0, half), slice(half, None))
    )
    fwd_in, bwd_in, cover = incoming_states(
        end_state(gated, rates),
        end_state(reversed_weighted, rates),
        rates,
        length,
        cover,
    )
    fwd_pieces = cover[0] + cover[1]
    bwd_pieces = cover[2] + cover[3]
    fwd_extra, bwd_extra = carried(fwd_in, bwd_in, scaled, rates, length)
    mixed = fwd_pieces.reshape(length, -1) + fwd_extra
    back = (bwd_pieces.reshape(length, -1) + bwd_extra)[::-1]
    output = (value_f * mixed).astype(jnp.bfloat16)
    grad_value = (cot_f * mixed).astype(jnp.bfloat16)
    grad_query = (back * key_f).astype(jnp.bfloat16)
    grad_key = (back * query_f).astype(jnp.bfloat16)
    return (output, grad_query, grad_key, grad_value)


def solution(mesh):
    return jax.shard_map(
        per_device,
        mesh=mesh,
        in_specs=(
            P("ctx", "chan"),
            P("ctx", "chan"),
            P("ctx", "chan"),
            P(None, "chan"),
            P(None, "chan"),
            P("ctx", "chan"),
        ),
        out_specs=(P("ctx", "chan"), P("ctx", "chan"), P("ctx", "chan"), P("ctx", "chan")),
        check_vma=False,
    )
```

```python
import jax
import jax.numpy as jnp
from jax import lax
from jax.experimental import pallas as pl
from jax.sharding import PartitionSpec as P

BLOCK = 64


def local_kernel(signal_ref, scaled_ref, rates_ref, out_ref):
    length, width = signal_ref.shape
    order = rates_ref.shape[0]
    lags = lax.broadcasted_iota(jnp.int32, (BLOCK, width), 0).astype(jnp.float32)
    lower = (
        lax.broadcasted_iota(jnp.int32, (BLOCK, BLOCK), 0)
        >= lax.broadcasted_iota(jnp.int32, (BLOCK, BLOCK), 1)
    ).astype(jnp.bfloat16)
    out_ref[...] = jnp.zeros(out_ref.shape, jnp.float32)

    def mode(m, carry):
        rate = rates_ref[pl.ds(m, 1), :]
        weight = scaled_ref[pl.ds(m, 1), :]
        rising = jnp.exp(rate * lags)
        falling = jnp.exp(-rate * lags)
        step_decay = jnp.exp(-rate)
        state = jnp.zeros((1, width), jnp.float32)
        for b in range(length // BLOCK):
            rows = pl.ds(b * BLOCK, BLOCK)
            lifted = rising * signal_ref[rows, :]
            high = lifted.astype(jnp.bfloat16)
            low = (lifted - high.astype(jnp.float32)).astype(jnp.bfloat16)
            summed = jnp.dot(lower, high, preferred_element_type=jnp.float32) + jnp.dot(
                lower, low, preferred_element_type=jnp.float32
            )
            states = falling * (summed + step_decay * state)
            out_ref[rows, :] += weight * states
            state = states[BLOCK - 1 : BLOCK, :]
        return carry

    lax.fori_loop(0, order, mode, 0)


def local_pass(signal, scaled, rates):
    length, width = signal.shape
    pieces = pl.pallas_call(
        local_kernel, out_shape=jax.ShapeDtypeStruct((length, width), jnp.float32)
    )(signal, scaled, rates)
    return pieces.reshape(length // BLOCK, BLOCK, width)


def carried_kernel(fwd_ref, bwd_ref, got_ref, into_ref, scaled_ref, rates_ref, fwd_out, bwd_out):
    length, width = fwd_out.shape
    order = rates_ref.shape[0]
    lags = lax.broadcasted_iota(jnp.int32, (BLOCK, width), 0).astype(jnp.float32) + 1.0
    fwd_out[...] = jnp.zeros(fwd_out.shape, jnp.float32)
    bwd_out[...] = jnp.zeros(bwd_out.shape, jnp.float32)

    def mode(m, carry):
        rate = rates_ref[pl.ds(m, 1), :]
        weight = scaled_ref[pl.ds(m, 1), :]
        fwd_in = fwd_ref[pl.ds(m, 1), :] + into_ref[0, pl.ds(m, 1), :] * got_ref[0, pl.ds(m, 1), :]
        bwd_in = bwd_ref[pl.ds(m, 1), :] + into_ref[1, pl.ds(m, 1), :] * got_ref[1, pl.ds(m, 1), :]
        fwd_weight = weight * fwd_in
        bwd_weight = weight * bwd_in
        after = jnp.exp(-rate * lags)
        for b in range(length // BLOCK):
            rows = pl.ds(b * BLOCK, BLOCK)
            start = jnp.exp(-rate * float(b * BLOCK))
            fwd_out[rows, :] += after * (fwd_weight * start)
            bwd_out[rows, :] += after * (bwd_weight * start)
        return carry

    lax.fori_loop(0, order, mode, 0)


def carried(fwd_in, bwd_in, last, scaled, rates, length):
    shape = jax.ShapeDtypeStruct((length, fwd_in.shape[1]), jnp.float32)
    return pl.pallas_call(carried_kernel, out_shape=(shape, shape))(
        fwd_in, bwd_in, last[0], last[1], scaled, rates
    )


def end_state(signal, rates):
    length, width = signal.shape
    part = 16
    lags = jnp.arange(part).astype(jnp.float32)
    inner = jnp.exp(-rates[None] * (part - 1.0 - lags)[:, None, None])
    outer = jnp.exp(-rates[None] * (part * (length // part - 1.0 - jnp.arange(length // part)))[:, None, None])
    rows = signal.reshape(length // part, part, 1, width)
    return jnp.sum(outer * jnp.sum(inner[None] * rows, axis=1), axis=0)


RINGS = (4, 8, 2)


def partner(place, span, count):
    sizes = RINGS if count == 4 * 8 * 2 else (count,)
    inner = count
    for size in sizes:
        inner //= size
        coord = (place // inner) % size
        if span < inner or span >= inner * size:
            continue
        bit = span // inner
        if size >= 4 and bit == size // 2:
            quarter = size // 4
            moved = coord + quarter if (coord // quarter) % 2 == 1 else coord - quarter
            return place + ((moved % size) - coord) * inner
        return place ^ span
    return place ^ span


def incoming_states(fwd_state, bwd_state, rates, length, cover):
    count = lax.axis_size("ctx")
    place = lax.axis_index("ctx")
    rounds = []
    span = 1
    while span < count:
        rounds.append(span)
        span *= 2
    slots = {span: k for k, span in enumerate(rounds[len(rounds) - len(cover) :])}
    cover = list(cover)
    fwd_total, bwd_total = fwd_state, bwd_state
    fwd_in = jnp.zeros_like(fwd_state)
    bwd_in = jnp.zeros_like(bwd_state)
    for span in rounds:
        got = lax.ppermute(
            jnp.stack([fwd_total, bwd_total]),
            "ctx",
            [(i, partner(i, span, count)) for i in range(count)],
        )
        if span in slots:
            got, cover[slots[span]] = lax.optimization_barrier((got, cover[slots[span]]))
        fwd_got, bwd_got = got[0], got[1]
        upper = (place // span) % 2 == 1
        offset = (place % span).astype(jnp.float32)
        fwd_weight = jnp.where(upper, jnp.exp(-rates * (length * offset)), 0.0)
        bwd_weight = jnp.where(upper, 0.0, jnp.exp(-rates * (length * (span - 1.0 - offset))))
        if 2 * span >= count:
            last = (got, jnp.stack([fwd_weight, bwd_weight]))
            break
        fwd_in = fwd_in + fwd_weight * fwd_got
        bwd_in = bwd_in + bwd_weight * bwd_got
        if 2 * span < count:
            whole = jnp.exp(-rates * (length * span))
            fwd_total = jnp.where(upper, whole * fwd_got + fwd_total, whole * fwd_total + fwd_got)
            bwd_total = jnp.where(upper, bwd_got + whole * bwd_total, bwd_total + whole * bwd_got)
    return fwd_in, bwd_in, last, tuple(cover)


def per_device(query, key_proj, value, residues, rates, cotangent):
    length = query.shape[0]
    query_f = query.astype(jnp.float32)
    key_f = key_proj.astype(jnp.float32)
    value_f = value.astype(jnp.float32)
    cot_f = cotangent.astype(jnp.float32)
    scaled = residues * jnp.sqrt(-jnp.expm1(-2.0 * rates))
    gated = lax.optimization_barrier((query_f * key_f).astype(jnp.bfloat16)).astype(jnp.float32)
    weighted = cot_f * value_f
    reversed_weighted = weighted[::-1]
    half = rates.shape[0] // 2
    cover = tuple(
        local_pass(signal, scaled[modes], rates[modes])
        for signal in (gated, reversed_weighted)
        for modes in (slice(0, half), slice(half, None))
    )
    fwd_in, bwd_in, last, cover = incoming_states(
        end_state(gated, rates),
        end_state(reversed_weighted, rates),
        rates,
        length,
        cover,
    )
    fwd_pieces = cover[0] + cover[1]
    bwd_pieces = cover[2] + cover[3]
    fwd_extra, bwd_extra = carried(fwd_in, bwd_in, last, scaled, rates, length)
    mixed = fwd_pieces.reshape(length, -1) + fwd_extra
    back = (bwd_pieces.reshape(length, -1) + bwd_extra)[::-1]
    output = (value_f * mixed).astype(jnp.bfloat16)
    grad_value = (cot_f * mixed).astype(jnp.bfloat16)
    grad_query = (back * key_f).astype(jnp.bfloat16)
    grad_key = (back * query_f).astype(jnp.bfloat16)
    return (output, grad_query, grad_key, grad_value)


def solution(mesh):
    return jax.shard_map(
        per_device,
        mesh=mesh,
        in_specs=(
            P("ctx", "chan"),
            P("ctx", "chan"),
            P("ctx", "chan"),
            P(None, "chan"),
            P(None, "chan"),
            P("ctx", "chan"),
        ),
        out_specs=(P("ctx", "chan"), P("ctx", "chan"), P("ctx", "chan"), P("ctx", "chan")),
        check_vma=False,
    )
```

```python
import jax
import jax.numpy as jnp
from jax import lax
from jax.experimental import pallas as pl
from jax.sharding import PartitionSpec as P

BLOCK = 64


def local_kernel(fwd_ref, bwd_ref, scaled_ref, rates_ref, fwd_out, bwd_out):
    length, width = fwd_ref.shape
    order = rates_ref.shape[0]
    lags = lax.broadcasted_iota(jnp.int32, (BLOCK, width), 0).astype(jnp.float32)
    lower = (
        lax.broadcasted_iota(jnp.int32, (BLOCK, BLOCK), 0)
        >= lax.broadcasted_iota(jnp.int32, (BLOCK, BLOCK), 1)
    ).astype(jnp.bfloat16)
    fwd_out[...] = jnp.zeros(fwd_out.shape, jnp.float32)
    bwd_out[...] = jnp.zeros(bwd_out.shape, jnp.float32)

    def mode(m, carry):
        rate = rates_ref[pl.ds(m, 1), :]
        weight = scaled_ref[pl.ds(m, 1), :]
        rising = jnp.exp(rate * lags)
        falling = jnp.exp(-rate * lags)
        step_decay = jnp.exp(-rate)
        for signal_ref, out_ref in ((fwd_ref, fwd_out), (bwd_ref, bwd_out)):
            state = jnp.zeros((1, width), jnp.float32)
            for b in range(length // BLOCK):
                rows = pl.ds(b * BLOCK, BLOCK)
                lifted = rising * signal_ref[rows, :]
                high = lifted.astype(jnp.bfloat16)
                low = (lifted - high.astype(jnp.float32)).astype(jnp.bfloat16)
                summed = jnp.dot(lower, high, preferred_element_type=jnp.float32) + jnp.dot(
                    lower, low, preferred_element_type=jnp.float32
                )
                states = falling * (summed + step_decay * state)
                out_ref[rows, :] += weight * states
                state = states[BLOCK - 1 : BLOCK, :]
        return carry

    lax.fori_loop(0, order, mode, 0)


def local_pass(fwd_signal, bwd_signal, scaled, rates):
    length, width = fwd_signal.shape
    shape = jax.ShapeDtypeStruct((length, width), jnp.float32)
    fwd_pieces, bwd_pieces = pl.pallas_call(local_kernel, out_shape=(shape, shape))(
        fwd_signal, bwd_signal, scaled, rates
    )
    return fwd_pieces, bwd_pieces


def carried_kernel(fwd_ref, bwd_ref, scaled_ref, rates_ref, fwd_out, bwd_out):
    length, width = fwd_out.shape
    order = rates_ref.shape[0]
    lags = lax.broadcasted_iota(jnp.int32, (BLOCK, width), 0).astype(jnp.float32) + 1.0
    fwd_out[...] = jnp.zeros(fwd_out.shape, jnp.float32)
    bwd_out[...] = jnp.zeros(bwd_out.shape, jnp.float32)

    def mode(m, carry):
        rate = rates_ref[pl.ds(m, 1), :]
        weight = scaled_ref[pl.ds(m, 1), :]
        fwd_weight = weight * fwd_ref[pl.ds(m, 1), :]
        bwd_weight = weight * bwd_ref[pl.ds(m, 1), :]
        after = jnp.exp(-rate * lags)
        for b in range(length // BLOCK):
            rows = pl.ds(b * BLOCK, BLOCK)
            start = jnp.exp(-rate * float(b * BLOCK))
            fwd_out[rows, :] += after * (fwd_weight * start)
            bwd_out[rows, :] += after * (bwd_weight * start)
        return carry

    lax.fori_loop(0, order, mode, 0)


def carried(fwd_in, bwd_in, scaled, rates, length):
    shape = jax.ShapeDtypeStruct((length, fwd_in.shape[1]), jnp.float32)
    return pl.pallas_call(carried_kernel, out_shape=(shape, shape))(fwd_in, bwd_in, scaled, rates)


def end_state(signal, rates):
    length, width = signal.shape
    part = 16
    lags = jnp.arange(part).astype(jnp.float32)
    inner = jnp.exp(-rates[None] * (part - 1.0 - lags)[:, None, None])
    outer = jnp.exp(-rates[None] * (part * (length // part - 1.0 - jnp.arange(length // part)))[:, None, None])
    rows = signal.reshape(length // part, part, 1, width)
    return jnp.sum(outer * jnp.sum(inner[None] * rows, axis=1), axis=0)


RINGS = (4, 8, 2)


def partner(place, span, count):
    sizes = RINGS if count == 4 * 8 * 2 else (count,)
    inner = count
    for size in sizes:
        inner //= size
        coord = (place // inner) % size
        if span < inner or span >= inner * size:
            continue
        bit = span // inner
        if size >= 4 and bit == size // 2:
            quarter = size // 4
            moved = coord + quarter if (coord // quarter) % 2 == 1 else coord - quarter
            return place + ((moved % size) - coord) * inner
        return place ^ span
    return place ^ span


def incoming_states(fwd_state, bwd_state, rates, length, cover):
    count = lax.axis_size("ctx")
    place = lax.axis_index("ctx")
    rounds = []
    span = 1
    while span < count:
        rounds.append(span)
        span *= 2
    slots = {span: k for k, span in enumerate(rounds[len(rounds) - len(cover) :])}
    cover = list(cover)
    fwd_total, bwd_total = fwd_state, bwd_state
    fwd_in = jnp.zeros_like(fwd_state)
    bwd_in = jnp.zeros_like(bwd_state)
    for span in rounds:
        got = lax.ppermute(
            jnp.stack([fwd_total, bwd_total]),
            "ctx",
            [(i, partner(i, span, count)) for i in range(count)],
        )
        if span in slots:
            got, cover[slots[span]] = lax.optimization_barrier((got, cover[slots[span]]))
        fwd_got, bwd_got = got[0], got[1]
        upper = (place // span) % 2 == 1
        offset = (place % span).astype(jnp.float32)
        fwd_in = fwd_in + jnp.where(upper, jnp.exp(-rates * (length * offset)), 0.0) * fwd_got
        bwd_in = bwd_in + jnp.where(
            upper, 0.0, jnp.exp(-rates * (length * (span - 1.0 - offset)))
        ) * bwd_got
        if 2 * span < count:
            whole = jnp.exp(-rates * (length * span))
            fwd_total = jnp.where(upper, whole * fwd_got + fwd_total, whole * fwd_total + fwd_got)
            bwd_total = jnp.where(upper, bwd_got + whole * bwd_total, bwd_total + whole * bwd_got)
    return fwd_in, bwd_in, tuple(cover)


def per_device(query, key_proj, value, residues, rates, cotangent):
    length = query.shape[0]
    query_f = query.astype(jnp.float32)
    key_f = key_proj.astype(jnp.float32)
    value_f = value.astype(jnp.float32)
    cot_f = cotangent.astype(jnp.float32)
    scaled = residues * jnp.sqrt(-jnp.expm1(-2.0 * rates))
    gated = lax.optimization_barrier((query_f * key_f).astype(jnp.bfloat16)).astype(jnp.float32)
    weighted = cot_f * value_f
    reversed_weighted = weighted[::-1]
    half = rates.shape[0] // 2
    cover = tuple(
        local_pass(gated, reversed_weighted, scaled[modes], rates[modes])
        for modes in (slice(0, half), slice(half, None))
    )
    fwd_in, bwd_in, cover = incoming_states(
        end_state(gated, rates),
        end_state(reversed_weighted, rates),
        rates,
        length,
        cover,
    )
    fwd_pieces = cover[0][0] + cover[1][0]
    bwd_pieces = cover[0][1] + cover[1][1]
    fwd_extra, bwd_extra = carried(fwd_in, bwd_in, scaled, rates, length)
    mixed = fwd_pieces + fwd_extra
    back = (bwd_pieces + bwd_extra)[::-1]
    output = (value_f * mixed).astype(jnp.bfloat16)
    grad_value = (cot_f * mixed).astype(jnp.bfloat16)
    grad_query = (back * key_f).astype(jnp.bfloat16)
    grad_key = (back * query_f).astype(jnp.bfloat16)
    return (output, grad_query, grad_key, grad_value)


def solution(mesh):
    return jax.shard_map(
        per_device,
        mesh=mesh,
        in_specs=(
            P("ctx", "chan"),
            P("ctx", "chan"),
            P("ctx", "chan"),
            P(None, "chan"),
            P(None, "chan"),
            P("ctx", "chan"),
        ),
        out_specs=(P("ctx", "chan"), P("ctx", "chan"), P("ctx", "chan"), P("ctx", "chan")),
        check_vma=False,
    )
```

```python
import jax
import jax.numpy as jnp
from jax import lax
from jax.experimental import pallas as pl
from jax.experimental.pallas import tpu as pltpu
from jax.sharding import PartitionSpec as P

BLOCK = 64


def local_kernel(fwd_ref, bwd_ref, scaled_ref, rates_ref, fwd_out, bwd_out):
    length, width = fwd_ref.shape
    order = rates_ref.shape[0]
    lags = lax.broadcasted_iota(jnp.int32, (BLOCK, width), 0).astype(jnp.float32)
    lower = (
        lax.broadcasted_iota(jnp.int32, (BLOCK, BLOCK), 0)
        >= lax.broadcasted_iota(jnp.int32, (BLOCK, BLOCK), 1)
    ).astype(jnp.bfloat16)
    fwd_out[...] = jnp.zeros(fwd_out.shape, jnp.float32)
    bwd_out[...] = jnp.zeros(bwd_out.shape, jnp.float32)

    def mode(m, carry):
        rate = rates_ref[pl.ds(m, 1), :]
        weight = scaled_ref[pl.ds(m, 1), :]
        rising = jnp.exp(rate * lags)
        falling = jnp.exp(-rate * lags)
        step_decay = jnp.exp(-rate)
        for signal_ref, out_ref in ((fwd_ref, fwd_out), (bwd_ref, bwd_out)):
            state = jnp.zeros((1, width), jnp.float32)
            for b in range(length // BLOCK):
                rows = pl.ds(b * BLOCK, BLOCK)
                lifted = rising * signal_ref[rows, :]
                high = lifted.astype(jnp.bfloat16)
                low = (lifted - high.astype(jnp.float32)).astype(jnp.bfloat16)
                summed = jnp.dot(lower, high, preferred_element_type=jnp.float32) + jnp.dot(
                    lower, low, preferred_element_type=jnp.float32
                )
                states = falling * (summed + step_decay * state)
                out_ref[rows, :] += weight * states
                state = states[BLOCK - 1 : BLOCK, :]
        return carry

    lax.fori_loop(0, order, mode, 0)


def local_pass(fwd_signal, bwd_signal, scaled, rates):
    length, width = fwd_signal.shape
    shape = jax.ShapeDtypeStruct((length, width), jnp.float32)
    fwd_pieces, bwd_pieces = pl.pallas_call(local_kernel, out_shape=(shape, shape))(
        fwd_signal, bwd_signal, scaled, rates
    )
    return fwd_pieces, bwd_pieces


def carried_kernel(
    fwd_ref, bwd_ref, scaled_ref, rates_ref, pieces_ref, value_ref, cot_ref,
    out_ref, grad_ref, bwd_out, fwd_out,
):
    length, width = fwd_out.shape
    order = rates_ref.shape[0]
    lags = lax.broadcasted_iota(jnp.int32, (BLOCK, width), 0).astype(jnp.float32) + 1.0
    fwd_out[...] = jnp.zeros(fwd_out.shape, jnp.float32)
    bwd_out[...] = jnp.zeros(bwd_out.shape, jnp.float32)

    def mode(m, carry):
        rate = rates_ref[pl.ds(m, 1), :]
        weight = scaled_ref[pl.ds(m, 1), :]
        fwd_weight = weight * fwd_ref[pl.ds(m, 1), :]
        bwd_weight = weight * bwd_ref[pl.ds(m, 1), :]
        after = jnp.exp(-rate * lags)
        for b in range(length // BLOCK):
            rows = pl.ds(b * BLOCK, BLOCK)
            start = jnp.exp(-rate * float(b * BLOCK))
            fwd_out[rows, :] += after * (fwd_weight * start)
            bwd_out[rows, :] += after * (bwd_weight * start)
        return carry

    lax.fori_loop(0, order, mode, 0)
    mixed = pieces_ref[...] + fwd_out[...]
    out_ref[...] = (value_ref[...].astype(jnp.float32) * mixed).astype(jnp.bfloat16)
    grad_ref[...] = (cot_ref[...].astype(jnp.float32) * mixed).astype(jnp.bfloat16)


def carried(fwd_in, bwd_in, scaled, rates, pieces, value, cot):
    length, width = pieces.shape
    half = jax.ShapeDtypeStruct((length, width), jnp.bfloat16)
    full = jax.ShapeDtypeStruct((length, width), jnp.float32)
    return pl.pallas_call(
        carried_kernel,
        out_shape=(half, half, full),
        scratch_shapes=[pltpu.VMEM((length, width), jnp.float32)],
    )(fwd_in, bwd_in, scaled, rates, pieces, value, cot)


def end_state(signal, rates):
    length, width = signal.shape
    part = 16
    lags = jnp.arange(part).astype(jnp.float32)
    inner = jnp.exp(-rates[None] * (part - 1.0 - lags)[:, None, None])
    outer = jnp.exp(-rates[None] * (part * (length // part - 1.0 - jnp.arange(length // part)))[:, None, None])
    rows = signal.reshape(length // part, part, 1, width)
    return jnp.sum(outer * jnp.sum(inner[None] * rows, axis=1), axis=0)


RINGS = (4, 8, 2)


def partner(place, span, count):
    sizes = RINGS if count == 4 * 8 * 2 else (count,)
    inner = count
    for size in sizes:
        inner //= size
        coord = (place // inner) % size
        if span < inner or span >= inner * size:
            continue
        bit = span // inner
        if size >= 4 and bit == size // 2:
            quarter = size // 4
            moved = coord + quarter if (coord // quarter) % 2 == 1 else coord - quarter
            return place + ((moved % size) - coord) * inner
        return place ^ span
    return place ^ span


def incoming_states(fwd_state, bwd_state, rates, length, cover):
    count = lax.axis_size("ctx")
    place = lax.axis_index("ctx")
    rounds = []
    span = 1
    while span < count:
        rounds.append(span)
        span *= 2
    slots = {span: k for k, span in enumerate(rounds[len(rounds) - len(cover) :])}
    cover = list(cover)
    fwd_total, bwd_total = fwd_state, bwd_state
    fwd_in = jnp.zeros_like(fwd_state)
    bwd_in = jnp.zeros_like(bwd_state)
    for span in rounds:
        got = lax.ppermute(
            jnp.stack([fwd_total, bwd_total]),
            "ctx",
            [(i, partner(i, span, count)) for i in range(count)],
        )
        if span in slots:
            got, cover[slots[span]] = lax.optimization_barrier((got, cover[slots[span]]))
        fwd_got, bwd_got = got[0], got[1]
        upper = (place // span) % 2 == 1
        offset = (place % span).astype(jnp.float32)
        fwd_in = fwd_in + jnp.where(upper, jnp.exp(-rates * (length * offset)), 0.0) * fwd_got
        bwd_in = bwd_in + jnp.where(
            upper, 0.0, jnp.exp(-rates * (length * (span - 1.0 - offset)))
        ) * bwd_got
        if 2 * span < count:
            whole = jnp.exp(-rates * (length * span))
            fwd_total = jnp.where(upper, whole * fwd_got + fwd_total, whole * fwd_total + fwd_got)
            bwd_total = jnp.where(upper, bwd_got + whole * bwd_total, bwd_total + whole * bwd_got)
    return fwd_in, bwd_in, tuple(cover)


def per_device(query, key_proj, value, residues, rates, cotangent):
    length = query.shape[0]
    query_f = query.astype(jnp.float32)
    key_f = key_proj.astype(jnp.float32)
    value_f = value.astype(jnp.float32)
    cot_f = cotangent.astype(jnp.float32)
    scaled = residues * jnp.sqrt(-jnp.expm1(-2.0 * rates))
    gated = lax.optimization_barrier((query_f * key_f).astype(jnp.bfloat16)).astype(jnp.float32)
    weighted = cot_f * value_f
    reversed_weighted = weighted[::-1]
    half = rates.shape[0] // 2
    cover = tuple(
        local_pass(gated, reversed_weighted, scaled[modes], rates[modes])
        for modes in (slice(0, half), slice(half, None))
    )
    fwd_in, bwd_in, cover = incoming_states(
        end_state(gated, rates),
        end_state(reversed_weighted, rates),
        rates,
        length,
        cover,
    )
    fwd_pieces = cover[0][0] + cover[1][0]
    bwd_pieces = cover[0][1] + cover[1][1]
    output, grad_value, bwd_extra = carried(
        fwd_in, bwd_in, scaled, rates, fwd_pieces, value, cotangent
    )
    back = (bwd_pieces + bwd_extra)[::-1]
    grad_query = (back * key_f).astype(jnp.bfloat16)
    grad_key = (back * query_f).astype(jnp.bfloat16)
    return (output, grad_query, grad_key, grad_value)


def solution(mesh):
    return jax.shard_map(
        per_device,
        mesh=mesh,
        in_specs=(
            P("ctx", "chan"),
            P("ctx", "chan"),
            P("ctx", "chan"),
            P(None, "chan"),
            P(None, "chan"),
            P("ctx", "chan"),
        ),
        out_specs=(P("ctx", "chan"), P("ctx", "chan"), P("ctx", "chan"), P("ctx", "chan")),
        check_vma=False,
    )
```

```python
import jax
import jax.numpy as jnp
from jax import lax
from jax.experimental import pallas as pl
from jax.sharding import PartitionSpec as P

BLOCK = 64


def local_kernel(fwd_ref, bwd_ref, scaled_ref, rates_ref, fwd_out, bwd_out):
    length, width = fwd_ref.shape
    order = rates_ref.shape[0]
    lags = lax.broadcasted_iota(jnp.int32, (BLOCK, width), 0).astype(jnp.float32)
    lower = (
        lax.broadcasted_iota(jnp.int32, (BLOCK, BLOCK), 0)
        >= lax.broadcasted_iota(jnp.int32, (BLOCK, BLOCK), 1)
    ).astype(jnp.bfloat16)
    fwd_out[...] = jnp.zeros(fwd_out.shape, jnp.float32)
    bwd_out[...] = jnp.zeros(bwd_out.shape, jnp.float32)

    def mode(m, carry):
        rate = rates_ref[pl.ds(m, 1), :]
        weight = scaled_ref[pl.ds(m, 1), :]
        rising = jnp.exp(rate * lags)
        falling = jnp.exp(-rate * lags)
        step_decay = jnp.exp(-rate)
        for signal_ref, out_ref in ((fwd_ref, fwd_out), (bwd_ref, bwd_out)):
            state = jnp.zeros((1, width), jnp.float32)
            for b in range(length // BLOCK):
                rows = pl.ds(b * BLOCK, BLOCK)
                lifted = rising * signal_ref[rows, :]
                high = lifted.astype(jnp.bfloat16)
                low = (lifted - high.astype(jnp.float32)).astype(jnp.bfloat16)
                summed = jnp.dot(lower, high, preferred_element_type=jnp.float32) + jnp.dot(
                    lower, low, preferred_element_type=jnp.float32
                )
                states = falling * (summed + step_decay * state)
                out_ref[rows, :] += weight * states
                state = states[BLOCK - 1 : BLOCK, :]
        return carry

    lax.fori_loop(0, order, mode, 0)


def local_pass(fwd_signal, bwd_signal, scaled, rates):
    length, width = fwd_signal.shape
    shape = jax.ShapeDtypeStruct((length, width), jnp.float32)
    fwd_pieces, bwd_pieces = pl.pallas_call(local_kernel, out_shape=(shape, shape))(
        fwd_signal, bwd_signal, scaled, rates
    )
    return fwd_pieces, bwd_pieces


def carried_kernel(fwd_ref, bwd_ref, scaled_ref, rates_ref, fwd_out, bwd_out):
    length, width = fwd_out.shape
    order = rates_ref.shape[0]
    lags = lax.broadcasted_iota(jnp.int32, (BLOCK, width), 0).astype(jnp.float32) + 1.0
    fwd_out[...] = jnp.zeros(fwd_out.shape, jnp.float32)
    bwd_out[...] = jnp.zeros(bwd_out.shape, jnp.float32)

    def mode(m, carry):
        rate = rates_ref[pl.ds(m, 1), :]
        weight = scaled_ref[pl.ds(m, 1), :]
        fwd_weight = weight * fwd_ref[pl.ds(m, 1), :]
        bwd_weight = weight * bwd_ref[pl.ds(m, 1), :]
        after = jnp.exp(-rate * lags)
        for b in range(length // BLOCK):
            rows = pl.ds(b * BLOCK, BLOCK)
            start = jnp.exp(-rate * float(b * BLOCK))
            fwd_out[rows, :] += after * (fwd_weight * start)
            bwd_out[rows, :] += after * (bwd_weight * start)
        return carry

    lax.fori_loop(0, order, mode, 0)


def carried(fwd_in, bwd_in, scaled, rates, length):
    shape = jax.ShapeDtypeStruct((length, fwd_in.shape[1]), jnp.float32)
    return pl.pallas_call(carried_kernel, out_shape=(shape, shape))(fwd_in, bwd_in, scaled, rates)


def end_state(signal, rates):
    length, width = signal.shape
    part = 16
    lags = jnp.arange(part).astype(jnp.float32)
    inner = jnp.exp(-rates[None] * (part - 1.0 - lags)[:, None, None])
    outer = jnp.exp(-rates[None] * (part * (length // part - 1.0 - jnp.arange(length // part)))[:, None, None])
    rows = signal.reshape(length // part, part, 1, width)
    return jnp.sum(outer * jnp.sum(inner[None] * rows, axis=1), axis=0)


RINGS = (4, 8, 2)


def partner(place, span, count):
    sizes = RINGS if count == 4 * 8 * 2 else (count,)
    inner = count
    for size in sizes:
        inner //= size
        coord = (place // inner) % size
        if span < inner or span >= inner * size:
            continue
        bit = span // inner
        if size >= 4 and bit == size // 2:
            quarter = size // 4
            moved = coord + quarter if (coord // quarter) % 2 == 1 else coord - quarter
            return place + ((moved % size) - coord) * inner
        return place ^ span
    return place ^ span


def incoming_states(fwd_state, bwd_state, rates, length, cover):
    count = lax.axis_size("ctx")
    place = lax.axis_index("ctx")
    rounds = []
    span = 1
    while span < count:
        rounds.append(span)
        span *= 2
    slots = {span: k for k, span in enumerate(rounds[len(rounds) - 2 * len(cover) + 1 :: 2])}
    cover = list(cover)
    fwd_total, bwd_total = fwd_state, bwd_state
    fwd_in = jnp.zeros_like(fwd_state)
    bwd_in = jnp.zeros_like(bwd_state)
    for span in rounds:
        got = lax.ppermute(
            jnp.stack([fwd_total, bwd_total]),
            "ctx",
            [(i, partner(i, span, count)) for i in range(count)],
        )
        if span in slots:
            got, cover[slots[span]] = lax.optimization_barrier((got, cover[slots[span]]))
        fwd_got, bwd_got = got[0], got[1]
        upper = (place // span) % 2 == 1
        offset = (place % span).astype(jnp.float32)
        fwd_in = fwd_in + jnp.where(upper, jnp.exp(-rates * (length * offset)), 0.0) * fwd_got
        bwd_in = bwd_in + jnp.where(
            upper, 0.0, jnp.exp(-rates * (length * (span - 1.0 - offset)))
        ) * bwd_got
        if 2 * span < count:
            whole = jnp.exp(-rates * (length * span))
            fwd_total = jnp.where(upper, whole * fwd_got + fwd_total, whole * fwd_total + fwd_got)
            bwd_total = jnp.where(upper, bwd_got + whole * bwd_total, bwd_total + whole * bwd_got)
    return fwd_in, bwd_in, tuple(cover)


def per_device(query, key_proj, value, residues, rates, cotangent):
    length = query.shape[0]
    query_f = query.astype(jnp.float32)
    key_f = key_proj.astype(jnp.float32)
    value_f = value.astype(jnp.float32)
    cot_f = cotangent.astype(jnp.float32)
    scaled = residues * jnp.sqrt(-jnp.expm1(-2.0 * rates))
    gated = lax.optimization_barrier((query_f * key_f).astype(jnp.bfloat16)).astype(jnp.float32)
    weighted = cot_f * value_f
    reversed_weighted = weighted[::-1]
    half = rates.shape[0] // 2
    cover = tuple(
        local_pass(gated, reversed_weighted, scaled[modes], rates[modes])
        for modes in (slice(0, half), slice(half, None))
    )
    fwd_in, bwd_in, cover = incoming_states(
        end_state(gated, rates),
        end_state(reversed_weighted, rates),
        rates,
        length,
        cover,
    )
    fwd_pieces = cover[0][0] + cover[1][0]
    bwd_pieces = cover[0][1] + cover[1][1]
    fwd_extra, bwd_extra = carried(fwd_in, bwd_in, scaled, rates, length)
    mixed = fwd_pieces + fwd_extra
    back = (bwd_pieces + bwd_extra)[::-1]
    output = (value_f * mixed).astype(jnp.bfloat16)
    grad_value = (cot_f * mixed).astype(jnp.bfloat16)
    grad_query = (back * key_f).astype(jnp.bfloat16)
    grad_key = (back * query_f).astype(jnp.bfloat16)
    return (output, grad_query, grad_key, grad_value)


def solution(mesh):
    return jax.shard_map(
        per_device,
        mesh=mesh,
        in_specs=(
            P("ctx", "chan"),
            P("ctx", "chan"),
            P("ctx", "chan"),
            P(None, "chan"),
            P(None, "chan"),
            P("ctx", "chan"),
        ),
        out_specs=(P("ctx", "chan"), P("ctx", "chan"), P("ctx", "chan"), P("ctx", "chan")),
        check_vma=False,
    )
```
